256 devices in a mesh: segment: 4 (over x), dp: 64 (over y, z, core).
Axes of the slice: x: 4, y: 4, z: 8, core: 2. Of those that a mesh axis runs over, the one named last changes fastest.
Arguments:
- tokens: bfloat16 [32768, 8192], P('dp', 'segment'), may hold values from -16 to 16
- block_values: bfloat16 [8192, 768], P('segment'), may hold values from -0.09375 to 0.09375
- column_blocks: int32 [128, 12], P('segment'), may hold values from 0 to 15, as said below
- counts: int32 [128], P('segment'), may hold values from 4 to 12, as said below
- cotangent: bfloat16 [32768, 1024], P(('dp', 'segment')), may hold values from -6 to 6
Outputs:
- activation: bfloat16 [32768, 1024], P(('dp', 'segment'))
- input_grad: bfloat16 [32768, 8192], P('dp', 'segment')
- weight_grad: float32 [8192, 768], P(('segment', 'dp'))
The draws below stay inside these ranges and needn't reach their ends.
Inputs may be any that keep to these rules, and one draw needn't show every extreme that they name: `column_blocks`: the first counts[r] entries of row r are distinct column blocks; entries at later slots are column blocks too and are ignored. `counts`: some row block uses all 12 slots.
All inputs are finite; a program needn't handle non-finite values.
Results may differ from the reference program's by a relative error of at most 0.001.
Values may be sent and summed in bfloat16 or wider, within the bound.
No kernel may reach another device: no remote copies, remote signals or barrier semaphores. Data moves between devices by JAX's collectives and lax.ppermute only.
A program may use at most 128 MiB of HBM per device.

```python
import jax
import jax.numpy as jnp
from jax import lax

D = 8192
KV = 1024
BLK = 64
KMAX = 12
TOKENS = 32768
REPLICAS = 64


def draw_column_blocks(key, part):
    row_keys = jax.random.split(jax.random.fold_in(key, 23), D // BLK)
    shuffled = jax.vmap(lambda one_key: jax.random.permutation(one_key, KV // BLK))(row_keys)
    return shuffled[:, :KMAX].astype(jnp.int32)


def draw_counts(key, part):
    counts_drawn = jax.random.randint(jax.random.fold_in(key, 11), (D // BLK,), KMAX // 3, KMAX + 1)
    where_full = jax.random.randint(jax.random.fold_in(key, 13), (), 0, D // BLK)
    return jnp.where(jnp.arange(D // BLK) == where_full, KMAX, counts_drawn).astype(jnp.int32)


def with_spikes(values, rng, source, target, blocks, factor):
    owner, partner = [(jnp.arange(values.shape[dim]) // (values.shape[dim] // blocks)).reshape([-1 if axis == dim else 1 for axis in range(values.ndim)]) for dim in (source, target)]
    chosen = jax.random.permutation(rng, blocks)[partner]
    strong = (owner == chosen) | (owner == (partner + blocks // 2) % blocks)
    return jnp.where(strong, factor * values, values)


def block_levels(stream_key, extent, pieces, least, top_value):
    level = 1.0
    for dim, parts in pieces:
        heights = jax.random.uniform(jax.random.fold_in(jax.random.fold_in(stream_key, 6), dim), (parts,), jnp.float32, least / len(pieces), top_value / len(pieces))
        level = level * jnp.repeat(jnp.exp(heights), extent[dim] // parts).reshape((-1,) + (1,) * (len(extent) - 1 - dim))
    return level


def noise(stream_key, extent, width, limit, pieces=(), kind=jnp.bfloat16):
    drawn = jax.random.normal(stream_key, extent, jnp.float32) * width
    if len(pieces) > 0:
        drawn = block_levels(stream_key, extent, pieces, -0.22, 0.18) * drawn
    return jnp.clip(drawn, min=-limit, max=limit).astype(kind)


def noise_with(stream_key, shape, scale, most, cuts, heavy, held_as=jnp.bfloat16):
    result = scale * jax.random.normal(stream_key, shape, jnp.float32)
    if cuts:
        result = result * block_levels(stream_key, shape, cuts, -0.22, 0.18)
    return jnp.clip(with_spikes(result, jax.random.fold_in(stream_key, 3), *heavy), -most, most).astype(held_as)


def setup_inputs(seed: int = 0) -> dict:
    key_of = jax.random.split(jax.random.key(seed), 6)
    tokens = noise_with(key_of[0], (TOKENS, D), 1.0, 16.0, ((0, 64), (1, 4)), (0, 1, 64, 4.0))
    block_values = noise(key_of[1], (D, KMAX * BLK), (D // 2) ** -0.5, 0.09375, ((0, 4),))
    column_blocks = draw_column_blocks(jax.random.fold_in(key_of[5], 71), 0)
    counts = draw_counts(jax.random.fold_in(key_of[5], 71), 0)
    cotangent = noise(key_of[4], (TOKENS, KV), 1.0, 6.0, ((0, 256),))
    return dict(tokens=tokens, block_values=block_values, column_blocks=column_blocks, counts=counts, cotangent=cotangent)


def block_onehot(column_blocks, counts, col_blocks):
    slots = column_blocks.shape[1]
    named = column_blocks[:, :, None] == jnp.arange(col_blocks, dtype=jnp.int32)[None, None, :]
    alive = jnp.arange(slots, dtype=jnp.int32)[None, :, None] < counts[:, None, None]
    return (named & alive).astype(jnp.float32)


def reference(tokens, block_values, column_blocks, counts, cotangent):
    row_blocks = D // BLK
    col_blocks = KV // BLK
    onehot = block_onehot(column_blocks, counts, col_blocks)
    blocks_view = block_values.astype(jnp.float32).reshape(row_blocks, BLK, KMAX, BLK)
    weight = jnp.einsum("bkc,bikj->bicj", onehot, blocks_view).reshape(D, KV).astype(jnp.bfloat16)
    preact = jnp.dot(tokens, weight, preferred_element_type=jnp.float32)
    activation = preact.astype(jnp.bfloat16)
    input_grad = jnp.dot(cotangent, weight.T, preferred_element_type=jnp.float32).astype(jnp.bfloat16)
    dense_grad = jnp.dot(tokens.T, cotangent, preferred_element_type=jnp.float32) / REPLICAS
    weight_grad = jnp.einsum("bkc,bicj->bikj", onehot, dense_grad.reshape(row_blocks, BLK, col_blocks, BLK),
                             precision=lax.Precision.HIGHEST).reshape(D, KMAX * BLK)
    return activation, input_grad, weight_grad
```

```python
import jax
import jax.numpy as jnp
from jax import lax
from jax.sharding import Mesh
from jax.sharding import PartitionSpec as P

DP_AXES = ("y", "z", "core")


def block_onehot(column_blocks, counts, col_blocks):
    slots = column_blocks.shape[1]
    named = column_blocks[:, :, None] == jnp.arange(col_blocks, dtype=jnp.int32)[None, None, :]
    alive = jnp.arange(slots, dtype=jnp.int32)[None, :, None] < counts[:, None, None]
    return named & alive


def slot_grad(tokens, cotangent_all, column_blocks, counts, block, replicas):
    local_rows, features = tokens.shape
    width = cotangent_all.shape[1]
    row_blocks, slots = column_blocks.shape
    col_blocks = width // block
    cot_rows = cotangent_all.T.reshape(col_blocks, block, local_rows)
    picked = jnp.take(cot_rows, column_blocks, axis=0, mode="clip")
    picked = picked.reshape(row_blocks, slots * block, local_rows)
    tok_rows = tokens.reshape(local_rows, row_blocks, block).transpose(1, 2, 0)
    grad = lax.dot_general(
        tok_rows, picked, (((2,), (2,)), ((0,), (0,))), preferred_element_type=jnp.float32
    )
    live = jnp.arange(slots, dtype=jnp.int32)[None, :] < counts[:, None]
    live = jnp.repeat(live, block, axis=1)[:, None, :]
    return jnp.where(live, grad / replicas, 0.0)


def per_device(tokens, block_values, column_blocks, counts, cotangent):
    local_rows, features = tokens.shape
    width = cotangent.shape[1]
    row_blocks, slots = column_blocks.shape
    block = features // row_blocks
    col_blocks = width // block
    sections = lax.axis_size("x")
    replicas = lax.axis_size(DP_AXES)
    n_y, n_z, n_core = (lax.axis_size(a) for a in DP_AXES)
    onehot = block_onehot(column_blocks, counts, col_blocks).astype(jnp.bfloat16)
    blocks_view = block_values.reshape(row_blocks, block, slots, block)
    weight = (
        jnp.einsum("bkc,bikj->bicj", onehot, blocks_view, preferred_element_type=jnp.float32)
        .astype(jnp.bfloat16)
        .reshape(features, width)
    )
    share_rows = local_rows // sections
    own_start = lax.axis_index("x") * share_rows
    partial_value = jnp.dot(tokens, weight, preferred_element_type=jnp.float32)
    preact_all = lax.psum(partial_value, "x")
    cotangent_all = lax.all_gather(cotangent, "x", axis=0, tiled=True)
    activation = lax.dynamic_slice_in_dim(preact_all, own_start, share_rows, 0).astype(jnp.bfloat16)
    picked = slot_grad(tokens, cotangent_all, column_blocks, counts, block, replicas)
    owned = features // replicas
    staged = (
        picked.reshape(n_y, n_z, n_core, owned, slots * block)
        .transpose(2, 1, 0, 3, 4)
        .reshape(features, slots * block)
    )
    staged = lax.psum_scatter(staged, "core", scatter_dimension=0, tiled=True)
    staged = lax.psum_scatter(staged, "z", scatter_dimension=0, tiled=True)
    weight_grad = lax.psum_scatter(staged, "y", scatter_dimension=0, tiled=True)
    input_grad = lax.dot_general(
        cotangent_all, weight, (((1,), (1,)), ((), ())), preferred_element_type=jnp.float32
    ).astype(jnp.bfloat16)
    return (activation, input_grad, weight_grad)


def solution(mesh):
    sections, replicas = mesh.devices.shape
    n_core = 2
    n_y = 4
    n_z = replicas // (n_y * n_core)
    fine = Mesh(mesh.devices.reshape(sections, n_y, n_z, n_core), ("x",) + DP_AXES)
    in_specs = (
        P(DP_AXES, "x"),
        P("x", None),
        P("x", None),
        P("x"),
        P(DP_AXES + ("x",), None),
    )
    out_specs = (P(DP_AXES + ("x",), None), P(DP_AXES, "x"), P(("x",) + DP_AXES, None))
    return jax.shard_map(
        per_device, mesh=fine, in_specs=in_specs, out_specs=out_specs, check_vma=False
    )
```

```python
import jax
import jax.numpy as jnp
from jax import lax
from jax.sharding import Mesh
from jax.sharding import PartitionSpec as P

DP_AXES = ("y", "z", "core")


def block_onehot(column_blocks, counts, col_blocks):
    slots = column_blocks.shape[1]
    named = column_blocks[:, :, None] == jnp.arange(col_blocks, dtype=jnp.int32)[None, None, :]
    alive = jnp.arange(slots, dtype=jnp.int32)[None, :, None] < counts[:, None, None]
    return named & alive


def slot_grad(tokens, cotangent_all, column_blocks, counts, block, replicas):
    local_rows, features = tokens.shape
    width = cotangent_all.shape[1]
    row_blocks, slots = column_blocks.shape
    col_blocks = width // block
    cot_rows = cotangent_all.T.reshape(col_blocks, block, local_rows)
    picked = jnp.take(cot_rows, column_blocks, axis=0, mode="clip")
    picked = picked.reshape(row_blocks, slots * block, local_rows)
    tok_rows = tokens.reshape(local_rows, row_blocks, block).transpose(1, 2, 0)
    grad = lax.dot_general(
        tok_rows, picked, (((2,), (2,)), ((0,), (0,))), preferred_element_type=jnp.float32
    )
    live = jnp.arange(slots, dtype=jnp.int32)[None, :] < counts[:, None]
    live = jnp.repeat(live, block, axis=1)[:, None, :]
    return jnp.where(live, grad / replicas, 0.0)


def ring_scatter(value, axis):
    n = lax.axis_size(axis)
    if n == 1:
        return value
    idx = lax.axis_index(axis)
    rows = value.shape[0] // n
    chunks = value.reshape(n, rows, value.shape[1])

    def take(j):
        return lax.dynamic_index_in_dim(chunks, j % n, 0, keepdims=False)

    if n == 2:
        return take(idx) + lax.ppermute(take(idx + 1), axis, [(0, 1), (1, 0)])
    half = value.shape[1] // 2
    fwd = [(i, (i + 1) % n) for i in range(n)]
    bwd = [(i, (i - 1) % n) for i in range(n)]
    a = take(idx - 1)[:, :half]
    b = take(idx + 1)[:, half:]
    for s in range(n - 1):
        a = lax.ppermute(a, axis, fwd) + take(idx - s - 2)[:, :half]
        b = lax.ppermute(b, axis, bwd) + take(idx + s + 2)[:, half:]
    return jnp.concatenate([a, b], axis=1)


def per_device(tokens, block_values, column_blocks, counts, cotangent):
    local_rows, features = tokens.shape
    width = cotangent.shape[1]
    row_blocks, slots = column_blocks.shape
    block = features // row_blocks
    col_blocks = width // block
    sections = lax.axis_size("x")
    replicas = lax.axis_size(DP_AXES)
    n_y, n_z, n_core = (lax.axis_size(a) for a in DP_AXES)
    onehot = block_onehot(column_blocks, counts, col_blocks).astype(jnp.bfloat16)
    blocks_view = block_values.reshape(row_blocks, block, slots, block)
    weight = (
        jnp.einsum("bkc,bikj->bicj", onehot, blocks_view, preferred_element_type=jnp.float32)
        .astype(jnp.bfloat16)
        .reshape(features, width)
    )
    partial_value = jnp.dot(tokens, weight, preferred_element_type=jnp.float32)
    preact_own = lax.psum_scatter(partial_value, "x", scatter_dimension=0, tiled=True)
    cotangent_all = lax.all_gather(cotangent, "x", axis=0, tiled=True)
    activation = preact_own.astype(jnp.bfloat16)
    picked = slot_grad(tokens, cotangent_all, column_blocks, counts, block, replicas)
    owned = features // replicas
    staged = (
        picked.reshape(n_y, n_z, n_core, owned, slots * block)
        .transpose(2, 1, 0, 3, 4)
        .reshape(features, slots * block)
    )
    staged = ring_scatter(staged, "core")
    staged = ring_scatter(staged, "z")
    weight_grad = ring_scatter(staged, "y")
    input_grad = lax.dot_general(
        cotangent_all, weight, (((1,), (1,)), ((), ())), preferred_element_type=jnp.float32
    ).astype(jnp.bfloat16)
    return (activation, input_grad, weight_grad)


def solution(mesh):
    sections, replicas = mesh.devices.shape
    n_core = 2
    n_y = 4
    n_z = replicas // (n_y * n_core)
    fine = Mesh(mesh.devices.reshape(sections, n_y, n_z, n_core), ("x",) + DP_AXES)
    in_specs = (
        P(DP_AXES, "x"),
        P("x", None),
        P("x", None),
        P("x"),
        P(DP_AXES + ("x",), None),
    )
    out_specs = (P(DP_AXES + ("x",), None), P(DP_AXES, "x"), P(("x",) + DP_AXES, None))
    return jax.shard_map(
        per_device, mesh=fine, in_specs=in_specs, out_specs=out_specs, check_vma=False
    )
```

```python
import jax
import jax.numpy as jnp
from jax import lax
from jax.sharding import Mesh
from jax.sharding import PartitionSpec as P

DP_AXES = ("y", "z", "core")


def block_onehot(column_blocks, counts, col_blocks):
    slots = column_blocks.shape[1]
    named = column_blocks[:, :, None] == jnp.arange(col_blocks, dtype=jnp.int32)[None, None, :]
    alive = jnp.arange(slots, dtype=jnp.int32)[None, :, None] < counts[:, None, None]
    return named & alive


def slot_grad(tokens, cotangent_all, column_blocks, counts, block, replicas):
    local_rows, features = tokens.shape
    width = cotangent_all.shape[1]
    row_blocks, slots = column_blocks.shape
    col_blocks = width // block
    cot_rows = cotangent_all.T.reshape(col_blocks, block, local_rows)
    picked = jnp.take(cot_rows, column_blocks, axis=0, mode="clip")
    picked = picked.reshape(row_blocks, slots * block, local_rows)
    tok_rows = tokens.reshape(local_rows, row_blocks, block).transpose(1, 2, 0)
    grad = lax.dot_general(
        tok_rows, picked, (((2,), (2,)), ((0,), (0,))), preferred_element_type=jnp.float32
    )
    live = jnp.arange(slots, dtype=jnp.int32)[None, :] < counts[:, None]
    live = jnp.repeat(live, block, axis=1)[:, None, :]
    return jnp.where(live, grad / replicas, 0.0)


def ring_scatter(value, axis):
    n = lax.axis_size(axis)
    if n == 1:
        return value
    idx = lax.axis_index(axis)
    rows = value.shape[0] // n
    chunks = value.reshape(n, rows, value.shape[1])

    def take(j):
        return lax.dynamic_index_in_dim(chunks, j % n, 0, keepdims=False)

    if n == 2:
        return take(idx) + lax.ppermute(take(idx + 1), axis, [(0, 1), (1, 0)])
    half = value.shape[1] // 2
    fwd = [(i, (i + 1) % n) for i in range(n)]
    bwd = [(i, (i - 1) % n) for i in range(n)]
    a = take(idx - 1)[:, :half]
    b = take(idx + 1)[:, half:]
    for s in range(n - 1):
        a = lax.ppermute(a, axis, fwd) + take(idx - s - 2)[:, :half]
        b = lax.ppermute(b, axis, bwd) + take(idx + s + 2)[:, half:]
    return jnp.concatenate([a, b], axis=1)


def per_device(tokens, block_values, column_blocks, counts, cotangent):
    local_rows, features = tokens.shape
    width = cotangent.shape[1]
    row_blocks, slots = column_blocks.shape
    block = features // row_blocks
    col_blocks = width // block
    replicas = lax.axis_size(DP_AXES)
    n_y, n_z, n_core = (lax.axis_size(a) for a in DP_AXES)
    onehot = block_onehot(column_blocks, counts, col_blocks).astype(jnp.bfloat16)
    blocks_view = block_values.reshape(row_blocks, block, slots, block)
    weight = (
        jnp.einsum("bkc,bikj->bicj", onehot, blocks_view, preferred_element_type=jnp.float32)
        .astype(jnp.bfloat16)
        .reshape(features, width)
    )
    partial_value = jnp.dot(tokens, weight, preferred_element_type=jnp.float32)
    cotangent_all = lax.all_gather(cotangent, "x", axis=0, tiled=True)
    partial_value, cotangent_all = lax.optimization_barrier((partial_value, cotangent_all))
    preact_own = lax.psum_scatter(partial_value, "x", scatter_dimension=0, tiled=True)
    activation = preact_own.astype(jnp.bfloat16)
    picked = slot_grad(tokens, cotangent_all, column_blocks, counts, block, replicas)
    owned = features // replicas
    staged = (
        picked.reshape(n_y, n_z, n_core, owned, slots * block)
        .transpose(2, 1, 0, 3, 4)
        .reshape(features, slots * block)
    )
    staged = ring_scatter(staged, "core")
    staged = ring_scatter(staged, "z")
    weight_grad = ring_scatter(staged, "y")
    input_grad = lax.dot_general(
        cotangent_all, weight, (((1,), (1,)), ((), ())), preferred_element_type=jnp.float32
    ).astype(jnp.bfloat16)
    return (activation, input_grad, weight_grad)


def solution(mesh):
    sections, replicas = mesh.devices.shape
    n_core = 2
    n_y = 4
    n_z = replicas // (n_y * n_core)
    fine = Mesh(mesh.devices.reshape(sections, n_y, n_z, n_core), ("x",) + DP_AXES)
    in_specs = (
        P(DP_AXES, "x"),
        P("x", None),
        P("x", None),
        P("x"),
        P(DP_AXES + ("x",), None),
    )
    out_specs = (P(DP_AXES + ("x",), None), P(DP_AXES, "x"), P(("x",) + DP_AXES, None))
    return jax.shard_map(
        per_device, mesh=fine, in_specs=in_specs, out_specs=out_specs, check_vma=False
    )
```

```python
import jax
import jax.numpy as jnp
from jax import lax
from jax.sharding import Mesh
from jax.sharding import PartitionSpec as P

DP_AXES = ("y", "z", "core")


def block_onehot(column_blocks, counts, col_blocks):
    slots = column_blocks.shape[1]
    named = column_blocks[:, :, None] == jnp.arange(col_blocks, dtype=jnp.int32)[None, None, :]
    alive = jnp.arange(slots, dtype=jnp.int32)[None, :, None] < counts[:, None, None]
    return named & alive


def slot_grad(tokens, cotangent_all, column_blocks, counts, block, replicas):
    local_rows, features = tokens.shape
    width = cotangent_all.shape[1]
    row_blocks, slots = column_blocks.shape
    col_blocks = width // block
    cot_rows = cotangent_all.T.reshape(col_blocks, block, local_rows)
    picked = jnp.take(cot_rows, column_blocks, axis=0, mode="clip")
    picked = picked.reshape(row_blocks, slots * block, local_rows)
    tok_rows = tokens.reshape(local_rows, row_blocks, block).transpose(1, 2, 0)
    grad = lax.dot_general(
        tok_rows, picked, (((2,), (2,)), ((0,), (0,))), preferred_element_type=jnp.float32
    )
    live = jnp.arange(slots, dtype=jnp.int32)[None, :] < counts[:, None]
    live = jnp.repeat(live, block, axis=1)[:, None, :]
    return jnp.where(live, grad / replicas, 0.0)


def ring_scatter(value, axis):
    n = lax.axis_size(axis)
    if n == 1:
        return value
    idx = lax.axis_index(axis)
    rows = value.shape[0] // n
    chunks = value.reshape(n, rows, value.shape[1])

    def take(j):
        return lax.dynamic_index_in_dim(chunks, j % n, 0, keepdims=False)

    if n == 2:
        return take(idx) + lax.ppermute(take(idx + 1), axis, [(0, 1), (1, 0)])
    half = value.shape[1] // 2
    fwd = [(i, (i + 1) % n) for i in range(n)]
    bwd = [(i, (i - 1) % n) for i in range(n)]
    a = take(idx - 1)[:, :half]
    b = take(idx + 1)[:, half:]
    for s in range(n - 1):
        a = lax.ppermute(a, axis, fwd) + take(idx - s - 2)[:, :half]
        b = lax.ppermute(b, axis, bwd) + take(idx + s + 2)[:, half:]
    return jnp.concatenate([a, b], axis=1)


def direct_scatter(value, axis):
    n = lax.axis_size(axis)
    idx = lax.axis_index(axis)
    rows = value.shape[0] // n
    chunks = value.reshape(n, rows, value.shape[1])

    def take(j):
        return lax.dynamic_index_in_dim(chunks, j % n, 0, keepdims=False)

    total = take(idx)
    for shift in range(1, n):
        perm = [(i, (i + shift) % n) for i in range(n)]
        total = total + lax.ppermute(take(idx + shift), axis, perm)
    return total


def per_device(tokens, block_values, column_blocks, counts, cotangent):
    local_rows, features = tokens.shape
    width = cotangent.shape[1]
    row_blocks, slots = column_blocks.shape
    block = features // row_blocks
    col_blocks = width // block
    replicas = lax.axis_size(DP_AXES)
    n_y, n_z, n_core = (lax.axis_size(a) for a in DP_AXES)
    onehot = block_onehot(column_blocks, counts, col_blocks).astype(jnp.bfloat16)
    blocks_view = block_values.reshape(row_blocks, block, slots, block)
    weight = (
        jnp.einsum("bkc,bikj->bicj", onehot, blocks_view, preferred_element_type=jnp.float32)
        .astype(jnp.bfloat16)
        .reshape(features, width)
    )
    partial_value = jnp.dot(tokens, weight, preferred_element_type=jnp.float32)
    cotangent_all = lax.all_gather(cotangent, "x", axis=0, tiled=True)
    partial_value, cotangent_all = lax.optimization_barrier((partial_value, cotangent_all))
    preact_own = lax.psum_scatter(partial_value, "x", scatter_dimension=0, tiled=True)
    activation = preact_own.astype(jnp.bfloat16)
    picked = slot_grad(tokens, cotangent_all, column_blocks, counts, block, replicas)
    owned = features // replicas
    staged = (
        picked.reshape(n_y, n_z, n_core, owned, slots * block)
        .transpose(2, 1, 0, 3, 4)
        .reshape(features, slots * block)
    )
    staged = ring_scatter(staged, "core")
    staged = ring_scatter(staged, "z")
    weight_grad = direct_scatter(staged, "y")
    input_grad = lax.dot_general(
        cotangent_all, weight, (((1,), (1,)), ((), ())), preferred_element_type=jnp.float32
    ).astype(jnp.bfloat16)
    return (activation, input_grad, weight_grad)


def solution(mesh):
    sections, replicas = mesh.devices.shape
    n_core = 2
    n_y = 4
    n_z = replicas // (n_y * n_core)
    fine = Mesh(mesh.devices.reshape(sections, n_y, n_z, n_core), ("x",) + DP_AXES)
    in_specs = (
        P(DP_AXES, "x"),
        P("x", None),
        P("x", None),
        P("x"),
        P(DP_AXES + ("x",), None),
    )
    out_specs = (P(DP_AXES + ("x",), None), P(DP_AXES, "x"), P(("x",) + DP_AXES, None))
    return jax.shard_map(
        per_device, mesh=fine, in_specs=in_specs, out_specs=out_specs, check_vma=False
    )
```

```python
import jax
import jax.numpy as jnp
from jax import lax
from jax.sharding import Mesh
from jax.sharding import PartitionSpec as P

DP_AXES = ("y", "z", "core")


def block_onehot(column_blocks, counts, col_blocks):
    slots = column_blocks.shape[1]
    named = column_blocks[:, :, None] == jnp.arange(col_blocks, dtype=jnp.int32)[None, None, :]
    alive = jnp.arange(slots, dtype=jnp.int32)[None, :, None] < counts[:, None, None]
    return named & alive


def slot_grad(tokens, cotangent_all, column_blocks, counts, block, replicas):
    local_rows, features = tokens.shape
    width = cotangent_all.shape[1]
    row_blocks, slots = column_blocks.shape
    col_blocks = width // block
    cot_rows = cotangent_all.T.reshape(col_blocks, block, local_rows)
    picked = jnp.take(cot_rows, column_blocks, axis=0, mode="clip")
    picked = picked.reshape(row_blocks, slots * block, local_rows)
    tok_rows = tokens.reshape(local_rows, row_blocks, block).transpose(1, 2, 0)
    grad = lax.dot_general(
        tok_rows, picked, (((2,), (2,)), ((0,), (0,))), preferred_element_type=jnp.float32
    )
    live = jnp.arange(slots, dtype=jnp.int32)[None, :] < counts[:, None]
    live = jnp.repeat(live, block, axis=1)[:, None, :]
    return jnp.where(live, grad / replicas, 0.0)


def ring_scatter(value, axis):
    n = lax.axis_size(axis)
    if n == 1:
        return value
    idx = lax.axis_index(axis)
    rows = value.shape[0] // n
    chunks = value.reshape(n, rows, value.shape[1])

    def take(j):
        return lax.dynamic_index_in_dim(chunks, j % n, 0, keepdims=False)

    if n == 2:
        return take(idx) + lax.ppermute(take(idx + 1), axis, [(0, 1), (1, 0)])
    half = value.shape[1] // 2
    fwd = [(i, (i + 1) % n) for i in range(n)]
    bwd = [(i, (i - 1) % n) for i in range(n)]
    a = take(idx - 1)[:, :half]
    b = take(idx + 1)[:, half:]
    for s in range(n - 1):
        a = lax.ppermute(a, axis, fwd) + take(idx - s - 2)[:, :half]
        b = lax.ppermute(b, axis, bwd) + take(idx + s + 2)[:, half:]
    return jnp.concatenate([a, b], axis=1)


def direct_scatter(value, axis):
    n = lax.axis_size(axis)
    idx = lax.axis_index(axis)
    rows = value.shape[0] // n
    chunks = value.reshape(n, rows, value.shape[1])

    def take(j):
        return lax.dynamic_index_in_dim(chunks, j % n, 0, keepdims=False)

    total = take(idx)
    for shift in range(1, n):
        perm = [(i, (i + shift) % n) for i in range(n)]
        total = total + lax.ppermute(take(idx + shift), axis, perm)
    return total


def meeting_scatter(value, axis):
    n = lax.axis_size(axis)
    idx = lax.axis_index(axis)
    rows = value.shape[0] // n
    chunks = value.reshape(n, rows, value.shape[1])

    def take(j):
        return lax.dynamic_index_in_dim(chunks, j % n, 0, keepdims=False)

    ahead = n // 2
    behind = n - 1 - ahead
    fwd = [(i, (i + 1) % n) for i in range(n)]
    bwd = [(i, (i - 1) % n) for i in range(n)]
    a = take(idx + ahead)
    for s in range(1, ahead + 1):
        a = lax.ppermute(a, axis, fwd) + take(idx + ahead - s)
    if behind == 0:
        return a
    b = take(idx - behind)
    for s in range(1, behind + 1):
        b = lax.ppermute(b, axis, bwd)
        if s < behind:
            b = b + take(idx - behind + s)
    return a + b


def per_device(tokens, block_values, column_blocks, counts, cotangent):
    local_rows, features = tokens.shape
    width = cotangent.shape[1]
    row_blocks, slots = column_blocks.shape
    block = features // row_blocks
    col_blocks = width // block
    replicas = lax.axis_size(DP_AXES)
    n_y, n_z, n_core = (lax.axis_size(a) for a in DP_AXES)
    onehot = block_onehot(column_blocks, counts, col_blocks).astype(jnp.bfloat16)
    blocks_view = block_values.reshape(row_blocks, block, slots, block)
    weight = (
        jnp.einsum("bkc,bikj->bicj", onehot, blocks_view, preferred_element_type=jnp.float32)
        .astype(jnp.bfloat16)
        .reshape(features, width)
    )
    partial_value = jnp.dot(tokens, weight, preferred_element_type=jnp.float32)
    cotangent_all = lax.all_gather(cotangent, "x", axis=0, tiled=True)
    partial_value, cotangent_all = lax.optimization_barrier((partial_value, cotangent_all))
    preact_own = lax.psum_scatter(partial_value, "x", scatter_dimension=0, tiled=True)
    activation = preact_own.astype(jnp.bfloat16)
    picked = slot_grad(tokens, cotangent_all, column_blocks, counts, block, replicas)
    owned = features // replicas
    staged = (
        picked.reshape(n_y, n_z, n_core, owned, slots * block)
        .transpose(2, 1, 0, 3, 4)
        .reshape(features, slots * block)
    )
    staged = ring_scatter(staged, "core")
    staged = meeting_scatter(staged, "z")
    weight_grad = direct_scatter(staged, "y")
    input_grad = lax.dot_general(
        cotangent_all, weight, (((1,), (1,)), ((), ())), preferred_element_type=jnp.float32
    ).astype(jnp.bfloat16)
    return (activation, input_grad, weight_grad)


def solution(mesh):
    sections, replicas = mesh.devices.shape
    n_core = 2
    n_y = 4
    n_z = replicas // (n_y * n_core)
    fine = Mesh(mesh.devices.reshape(sections, n_y, n_z, n_core), ("x",) + DP_AXES)
    in_specs = (
        P(DP_AXES, "x"),
        P("x", None),
        P("x", None),
        P("x"),
        P(DP_AXES + ("x",), None),
    )
    out_specs = (P(DP_AXES + ("x",), None), P(DP_AXES, "x"), P(("x",) + DP_AXES, None))
    return jax.shard_map(
        per_device, mesh=fine, in_specs=in_specs, out_specs=out_specs, check_vma=False
    )
```

```python
import jax
import jax.numpy as jnp
from jax import lax
from jax.sharding import Mesh
from jax.sharding import PartitionSpec as P

DP_AXES = ("y", "z", "core")


def block_onehot(column_blocks, counts, col_blocks):
    slots = column_blocks.shape[1]
    named = column_blocks[:, :, None] == jnp.arange(col_blocks, dtype=jnp.int32)[None, None, :]
    alive = jnp.arange(slots, dtype=jnp.int32)[None, :, None] < counts[:, None, None]
    return named & alive


def slot_grad(tokens, cotangent_all, column_blocks, counts, block, replicas):
    local_rows, features = tokens.shape
    width = cotangent_all.shape[1]
    row_blocks, slots = column_blocks.shape
    col_blocks = width // block
    cot_rows = cotangent_all.T.reshape(col_blocks, block, local_rows)
    picked = jnp.take(cot_rows, column_blocks, axis=0, mode="clip")
    picked = picked.reshape(row_blocks, slots * block, local_rows)
    tok_rows = tokens.reshape(local_rows, row_blocks, block).transpose(1, 2, 0)
    grad = lax.dot_general(
        tok_rows, picked, (((2,), (2,)), ((0,), (0,))), preferred_element_type=jnp.float32
    )
    live = jnp.arange(slots, dtype=jnp.int32)[None, :] < counts[:, None]
    live = jnp.repeat(live, block, axis=1)[:, None, :]
    return jnp.where(live, grad / replicas, 0.0)


def ring_scatter(value, axis):
    n = lax.axis_size(axis)
    if n == 1:
        return value
    idx = lax.axis_index(axis)
    rows = value.shape[0] // n
    chunks = value.reshape(n, rows, value.shape[1])

    def take(j):
        return lax.dynamic_index_in_dim(chunks, j % n, 0, keepdims=False)

    if n == 2:
        return take(idx) + lax.ppermute(take(idx + 1), axis, [(0, 1), (1, 0)])
    half = value.shape[1] // 2
    fwd = [(i, (i + 1) % n) for i in range(n)]
    bwd = [(i, (i - 1) % n) for i in range(n)]
    a = take(idx - 1)[:, :half]
    b = take(idx + 1)[:, half:]
    for s in range(n - 1):
        a = lax.ppermute(a, axis, fwd) + take(idx - s - 2)[:, :half]
        b = lax.ppermute(b, axis, bwd) + take(idx + s + 2)[:, half:]
    return jnp.concatenate([a, b], axis=1)


def direct_scatter(value, axis):
    n = lax.axis_size(axis)
    idx = lax.axis_index(axis)
    rows = value.shape[0] // n
    chunks = value.reshape(n, rows, value.shape[1])

    def take(j):
        return lax.dynamic_index_in_dim(chunks, j % n, 0, keepdims=False)

    total = take(idx)
    for shift in range(1, n):
        perm = [(i, (i + shift) % n) for i in range(n)]
        total = total + lax.ppermute(take(idx + shift), axis, perm)
    return total


def meeting_scatter(value, axis):
    n = lax.axis_size(axis)
    idx = lax.axis_index(axis)
    rows = value.shape[0] // n
    chunks = value.reshape(n, rows, value.shape[1])

    def take(j):
        return lax.dynamic_index_in_dim(chunks, j % n, 0, keepdims=False)

    ahead = n // 2
    behind = n - 1 - ahead
    fwd = [(i, (i + 1) % n) for i in range(n)]
    bwd = [(i, (i - 1) % n) for i in range(n)]
    a = take(idx + ahead)
    for s in range(1, ahead + 1):
        a = lax.ppermute(a, axis, fwd) + take(idx + ahead - s)
    if behind == 0:
        return a
    b = take(idx - behind)
    for s in range(1, behind + 1):
        b = lax.ppermute(b, axis, bwd)
        if s < behind:
            b = b + take(idx - behind + s)
    return a + b


def per_device(tokens, block_values, column_blocks, counts, cotangent):
    local_rows, features = tokens.shape
    width = cotangent.shape[1]
    row_blocks, slots = column_blocks.shape
    block = features // row_blocks
    col_blocks = width // block
    replicas = lax.axis_size(DP_AXES)
    n_y, n_z, n_core = (lax.axis_size(a) for a in DP_AXES)
    onehot = block_onehot(column_blocks, counts, col_blocks).astype(jnp.bfloat16)
    blocks_view = block_values.reshape(row_blocks, block, slots, block)
    weight = (
        jnp.einsum("bkc,bikj->bicj", onehot, blocks_view, preferred_element_type=jnp.float32)
        .astype(jnp.bfloat16)
        .reshape(features, width)
    )
    cotangent_all = lax.all_gather(cotangent, "x", axis=0, tiled=True)
    weight, cotangent_all = lax.optimization_barrier((weight, cotangent_all))
    partial_value = jnp.dot(tokens, weight, preferred_element_type=jnp.float32)
    preact_own = lax.psum_scatter(partial_value, "x", scatter_dimension=0, tiled=True)
    activation = preact_own.astype(jnp.bfloat16)
    picked = slot_grad(tokens, cotangent_all, column_blocks, counts, block, replicas)
    owned = features // replicas
    staged = (
        picked.reshape(n_y, n_z, n_core, owned, slots * block)
        .transpose(2, 1, 0, 3, 4)
        .reshape(features, slots * block)
    )
    staged = ring_scatter(staged, "core")
    staged = meeting_scatter(staged, "z")
    weight_grad = direct_scatter(staged, "y")
    input_grad = lax.dot_general(
        cotangent_all, weight, (((1,), (1,)), ((), ())), preferred_element_type=jnp.float32
    ).astype(jnp.bfloat16)
    return (activation, input_grad, weight_grad)


def solution(mesh):
    sections, replicas = mesh.devices.shape
    n_core = 2
    n_y = 4
    n_z = replicas // (n_y * n_core)
    fine = Mesh(mesh.devices.reshape(sections, n_y, n_z, n_core), ("x",) + DP_AXES)
    in_specs = (
        P(DP_AXES, "x"),
        P("x", None),
        P("x", None),
        P("x"),
        P(DP_AXES + ("x",), None),
    )
    out_specs = (P(DP_AXES + ("x",), None), P(DP_AXES, "x"), P(("x",) + DP_AXES, None))
    return jax.shard_map(
        per_device, mesh=fine, in_specs=in_specs, out_specs=out_specs, check_vma=False
    )
```

```python
import jax
import jax.numpy as jnp
from jax import lax
from jax.sharding import Mesh
from jax.sharding import PartitionSpec as P

DP_AXES = ("y", "z", "core")


def block_onehot(column_blocks, counts, col_blocks):
    slots = column_blocks.shape[1]
    named = column_blocks[:, :, None] == jnp.arange(col_blocks, dtype=jnp.int32)[None, None, :]
    alive = jnp.arange(slots, dtype=jnp.int32)[None, :, None] < counts[:, None, None]
    return named & alive


def slot_grad(tokens, cotangent_all, column_blocks, counts, block, replicas):
    local_rows, features = tokens.shape
    width = cotangent_all.shape[1]
    row_blocks, slots = column_blocks.shape
    col_blocks = width // block
    cot_rows = cotangent_all.T.reshape(col_blocks, block, local_rows)
    picked = jnp.take(cot_rows, column_blocks, axis=0, mode="clip")
    picked = picked.reshape(row_blocks, slots * block, local_rows)
    tok_rows = tokens.reshape(local_rows, row_blocks, block).transpose(1, 2, 0)
    grad = lax.dot_general(
        tok_rows, picked, (((2,), (2,)), ((0,), (0,))), preferred_element_type=jnp.float32
    )
    live = jnp.arange(slots, dtype=jnp.int32)[None, :] < counts[:, None]
    live = jnp.repeat(live, block, axis=1)[:, None, :]
    return jnp.where(live, grad / replicas, 0.0)


def ring_scatter(value, axis):
    n = lax.axis_size(axis)
    if n == 1:
        return value
    idx = lax.axis_index(axis)
    rows = value.shape[0] // n
    chunks = value.reshape(n, rows, value.shape[1])

    def take(j):
        return lax.dynamic_index_in_dim(chunks, j % n, 0, keepdims=False)

    if n == 2:
        return take(idx) + lax.ppermute(take(idx + 1), axis, [(0, 1), (1, 0)])
    half = value.shape[1] // 2
    fwd = [(i, (i + 1) % n) for i in range(n)]
    bwd = [(i, (i - 1) % n) for i in range(n)]
    a = take(idx - 1)[:, :half]
    b = take(idx + 1)[:, half:]
    for s in range(n - 1):
        a = lax.ppermute(a, axis, fwd) + take(idx - s - 2)[:, :half]
        b = lax.ppermute(b, axis, bwd) + take(idx + s + 2)[:, half:]
    return jnp.concatenate([a, b], axis=1)


def direct_scatter(value, axis):
    n = lax.axis_size(axis)
    idx = lax.axis_index(axis)
    rows = value.shape[0] // n
    chunks = value.reshape(n, rows, value.shape[1])

    def take(j):
        return lax.dynamic_index_in_dim(chunks, j % n, 0, keepdims=False)

    total = take(idx)
    for shift in range(1, n):
        perm = [(i, (i + shift) % n) for i in range(n)]
        total = total + lax.ppermute(take(idx + shift), axis, perm)
    return total


def meeting_scatter(value, axis):
    n = lax.axis_size(axis)
    idx = lax.axis_index(axis)
    rows = value.shape[0] // n
    chunks = value.reshape(n, rows, value.shape[1])

    def take(j):
        return lax.dynamic_index_in_dim(chunks, j % n, 0, keepdims=False)

    ahead = n // 2
    behind = n - 1 - ahead
    fwd = [(i, (i + 1) % n) for i in range(n)]
    bwd = [(i, (i - 1) % n) for i in range(n)]
    a = take(idx + ahead)
    for s in range(1, ahead + 1):
        a = lax.ppermute(a, axis, fwd) + take(idx + ahead - s)
    if behind == 0:
        return a
    b = take(idx - behind)
    for s in range(1, behind + 1):
        b = lax.ppermute(b, axis, bwd)
        if s < behind:
            b = b + take(idx - behind + s)
    return a + b


def per_device(tokens, block_values, column_blocks, counts, cotangent):
    local_rows, features = tokens.shape
    width = cotangent.shape[1]
    row_blocks, slots = column_blocks.shape
    block = features // row_blocks
    col_blocks = width // block
    replicas = lax.axis_size(DP_AXES)
    n_y, n_z, n_core = (lax.axis_size(a) for a in DP_AXES)
    onehot = block_onehot(column_blocks, counts, col_blocks).astype(jnp.bfloat16)
    blocks_view = block_values.reshape(row_blocks, block, slots, block)
    weight = (
        jnp.einsum("bkc,bikj->bicj", onehot, blocks_view, preferred_element_type=jnp.float32)
        .astype(jnp.bfloat16)
        .reshape(features, width)
    )
    cotangent_all = lax.all_gather(cotangent, "x", axis=0, tiled=True)
    weight, cotangent_all = lax.optimization_barrier((weight, cotangent_all))
    partial_value = jnp.dot(tokens, weight, preferred_element_type=jnp.float32)
    preact_own = lax.psum_scatter(partial_value, "x", scatter_dimension=0, tiled=True)
    activation = preact_own.astype(jnp.bfloat16)
    picked = slot_grad(tokens, cotangent_all, column_blocks, counts, block, replicas)
    owned = features // replicas
    staged = (
        picked.reshape(n_y, n_z, n_core, owned, slots * block)
        .transpose(2, 0, 1, 3, 4)
        .reshape(features, slots * block)
    )
    staged = ring_scatter(staged, "core")
    staged = direct_scatter(staged, "y")
    weight_grad = meeting_scatter(staged, "z")
    input_grad = lax.dot_general(
        cotangent_all, weight, (((1,), (1,)), ((), ())), preferred_element_type=jnp.float32
    ).astype(jnp.bfloat16)
    return (activation, input_grad, weight_grad)


def solution(mesh):
    sections, replicas = mesh.devices.shape
    n_core = 2
    n_y = 4
    n_z = replicas // (n_y * n_core)
    fine = Mesh(mesh.devices.reshape(sections, n_y, n_z, n_core), ("x",) + DP_AXES)
    in_specs = (
        P(DP_AXES, "x"),
        P("x", None),
        P("x", None),
        P("x"),
        P(DP_AXES + ("x",), None),
    )
    out_specs = (P(DP_AXES + ("x",), None), P(DP_AXES, "x"), P(("x",) + DP_AXES, None))
    return jax.shard_map(
        per_device, mesh=fine, in_specs=in_specs, out_specs=out_specs, check_vma=False
    )
```

```python
import jax
import jax.numpy as jnp
from jax import lax
from jax.sharding import Mesh
from jax.sharding import PartitionSpec as P

DP_AXES = ("y", "z", "core")


def block_onehot(column_blocks, counts, col_blocks):
    slots = column_blocks.shape[1]
    named = column_blocks[:, :, None] == jnp.arange(col_blocks, dtype=jnp.int32)[None, None, :]
    alive = jnp.arange(slots, dtype=jnp.int32)[None, :, None] < counts[:, None, None]
    return named & alive


def slot_grad(tokens, cotangent_all, column_blocks, counts, block, replicas):
    local_rows, features = tokens.shape
    width = cotangent_all.shape[1]
    row_blocks, slots = column_blocks.shape
    col_blocks = width // block
    cot_rows = cotangent_all.T.reshape(col_blocks, block, local_rows)
    picked = jnp.take(cot_rows, column_blocks, axis=0, mode="clip")
    picked = picked.reshape(row_blocks, slots * block, local_rows)
    tok_rows = tokens.reshape(local_rows, row_blocks, block).transpose(1, 2, 0)
    grad = lax.dot_general(
        tok_rows, picked, (((2,), (2,)), ((0,), (0,))), preferred_element_type=jnp.float32
    )
    live = jnp.arange(slots, dtype=jnp.int32)[None, :] < counts[:, None]
    live = jnp.repeat(live, block, axis=1)[:, None, :]
    return jnp.where(live, grad / replicas, 0.0)


def ring_scatter(value, axis, dim):
    idx = lax.axis_index(axis)
    mine = lax.dynamic_index_in_dim(value, idx, dim, keepdims=False)
    other = lax.dynamic_index_in_dim(value, 1 - idx, dim, keepdims=False)
    return mine + lax.ppermute(other, axis, [(0, 1), (1, 0)])


def direct_scatter(value, axis):
    n = lax.axis_size(axis)
    idx = lax.axis_index(axis)
    rows = value.shape[0] // n
    chunks = value.reshape(n, rows, value.shape[1])

    def take(j):
        return lax.dynamic_index_in_dim(chunks, j % n, 0, keepdims=False)

    total = take(idx)
    for shift in range(1, n):
        perm = [(i, (i + shift) % n) for i in range(n)]
        total = total + lax.ppermute(take(idx + shift), axis, perm)
    return total


def meeting_scatter(value, axis, dim):
    n = lax.axis_size(axis)
    idx = lax.axis_index(axis)

    def take(j):
        return lax.dynamic_index_in_dim(value, j % n, dim, keepdims=False)

    ahead = n // 2
    behind = n - 1 - ahead
    fwd = [(i, (i + 1) % n) for i in range(n)]
    bwd = [(i, (i - 1) % n) for i in range(n)]
    a = take(idx + ahead)
    for s in range(1, ahead + 1):
        a = lax.ppermute(a, axis, fwd) + take(idx + ahead - s)
    if behind == 0:
        return a
    b = take(idx - behind)
    for s in range(1, behind + 1):
        b = lax.ppermute(b, axis, bwd)
        if s < behind:
            b = b + take(idx - behind + s)
    return a + b


def per_device(tokens, block_values, column_blocks, counts, cotangent):
    local_rows, features = tokens.shape
    width = cotangent.shape[1]
    row_blocks, slots = column_blocks.shape
    block = features // row_blocks
    col_blocks = width // block
    replicas = lax.axis_size(DP_AXES)
    n_y, n_z, n_core = (lax.axis_size(a) for a in DP_AXES)
    onehot = block_onehot(column_blocks, counts, col_blocks).astype(jnp.bfloat16)
    blocks_view = block_values.reshape(row_blocks, block, slots, block)
    weight = (
        jnp.einsum("bkc,bikj->bicj", onehot, blocks_view, preferred_element_type=jnp.float32)
        .astype(jnp.bfloat16)
        .reshape(features, width)
    )
    cotangent_all = lax.all_gather(cotangent, "x", axis=0, tiled=True)
    weight, cotangent_all = lax.optimization_barrier((weight, cotangent_all))
    partial_value = jnp.dot(tokens, weight, preferred_element_type=jnp.float32)
    preact_own = lax.psum_scatter(partial_value, "x", scatter_dimension=0, tiled=True)
    activation = preact_own.astype(jnp.bfloat16)
    picked = slot_grad(tokens, cotangent_all, column_blocks, counts, block, replicas)
    owned = features // replicas
    staged = picked.reshape(n_y * n_z, n_core, owned, slots * block)
    staged = ring_scatter(staged, "core", 1)
    staged = meeting_scatter(staged.reshape(n_y, n_z, owned, slots * block), "z", 1)
    weight_grad = direct_scatter(staged.reshape(n_y * owned, slots * block), "y")
    input_grad = lax.dot_general(
        cotangent_all, weight, (((1,), (1,)), ((), ())), preferred_element_type=jnp.float32
    ).astype(jnp.bfloat16)
    return (activation, input_grad, weight_grad)


def solution(mesh):
    sections, replicas = mesh.devices.shape
    n_core = 2
    n_y = 4
    n_z = replicas // (n_y * n_core)
    fine = Mesh(mesh.devices.reshape(sections, n_y, n_z, n_core), ("x",) + DP_AXES)
    in_specs = (
        P(DP_AXES, "x"),
        P("x", None),
        P("x", None),
        P("x"),
        P(DP_AXES + ("x",), None),
    )
    out_specs = (P(DP_AXES + ("x",), None), P(DP_AXES, "x"), P(("x",) + DP_AXES, None))
    return jax.shard_map(
        per_device, mesh=fine, in_specs=in_specs, out_specs=out_specs, check_vma=False
    )
```
